256 devices in a mesh: mem: 32 (over z, x), pipe: 4 (over y), dp: 2 (over core).
Axes of the slice: x: 4, y: 4, z: 8, core: 2. Of those that a mesh axis runs over, the one named last changes fastest.
Arguments:
- values: bfloat16 [32768, 4096], P(('dp', 'mem'), 'pipe'), parts along dimension 0, may hold values from -6 to 6
- cotangent: bfloat16 [8192, 4096], P(('dp', 'mem'), 'pipe'), parts along dimension 0, may hold values from -6 to 6
- scores: float32 [8192, 4, 32], P(('dp', 'mem')), parts along dimension 0, may hold values from -8 to 410, as said below
- row_lists: int32 [64, 32, 128], P(('dp', 'mem')), parts along dimension 0, may hold values from -1 to 511, as said below
- sel_slot: int32 [8192, 4, 32], P(('dp', 'mem')), parts along dimension 0, may hold values from 0 to 4095, as said below
Outputs:
- mem_out: bfloat16 [8192, 4096], P(('dp', 'mem'), 'pipe'), parts along dimension 0
- grad_values: bfloat16 [32768, 4096], P(('dp', 'mem'), 'pipe'), parts along dimension 0
- grad_scores: float32 [8192, 4, 32], P(('dp', 'mem')), parts along dimension 0
The draws below stay inside these ranges and needn't reach their ends.
There are 2 independent parts, one for each index of `dp`. The reference program is written for one: setup_inputs(seed, part) draws one part's arguments, and reference() takes and returns one part's arrays. A program takes and returns all parts, laid end to end along the dimension named above; each array names one. Nothing has to cross between parts.
Inputs may be any that keep to these rules, and one draw needn't show every extreme that they name: `row_lists`: each entry is a row of the owner's shard, or -1 for an empty slot; the rows of one block are distinct and its empty slots come last; in every draw some owner receives full blocks of 128 rows from every device. `sel_slot`: each entry names a slot of the request blocks of the token's own mem index, and that slot holds a row; the 32 entries of one token and head are distinct. `scores`: scores are finite.
All inputs are finite; a program needn't handle non-finite values.
Results may differ from the reference program's by a relative error of at most 0.013.
Values may be sent and summed in bfloat16 or wider, within the bound.
No kernel may reach another device: no remote copies, remote signals or barrier semaphores. Data moves between devices by JAX's collectives and lax.ppermute only.
A program may use at most 128 MiB of HBM per device.

```python
import jax
import jax.numpy as jnp
from jax import lax

D = 4096
HEADS = 4
TOPK = 32
CAP = 128
TOK_DEV = 128
ROWS_DEV = 512
OWNERS = 32
TOKENS = 4096
ROWS = 16384


def block_counts(key):
    base = jax.random.fold_in(key, 7)
    hot = max(1, OWNERS // 8)
    order = jax.random.permutation(jax.random.fold_in(base, 1), OWNERS)
    owner_ids = jnp.arange(OWNERS, dtype=jnp.int32)
    is_hot = jnp.any(owner_ids[:, None] == order[None, :hot], axis=1)
    counts = jax.random.randint(jax.random.fold_in(base, 2), (OWNERS, OWNERS), max(1, CAP // 8), CAP // 2 + 1)
    return jnp.where(is_hot[None, :], CAP, counts).astype(jnp.int32)


def draw_row_lists(key, part):
    counts = block_counts(key)
    ranks = jax.random.randint(jax.random.fold_in(key, 3), (OWNERS, OWNERS, ROWS_DEV), 0, 4096)
    keyed = ranks * ROWS_DEV + jnp.arange(ROWS_DEV, dtype=jnp.int32)
    order = jnp.argsort(keyed, axis=-1)[..., :CAP].astype(jnp.int32)
    valid = jnp.arange(CAP, dtype=jnp.int32)[None, None, :] < counts[..., None]
    return jnp.where(valid, order, -1).astype(jnp.int32)


def draw_sel_slot(key, part):
    counts = block_counts(key)
    slot_ids = jnp.arange(OWNERS * CAP, dtype=jnp.int32)
    valid = (slot_ids % CAP)[None, :] < jnp.repeat(counts, CAP, axis=1)
    pick_key = jax.random.fold_in(key, 5)

    def one_sender(sender):
        ranks = jax.random.randint(jax.random.fold_in(pick_key, sender), (TOK_DEV * HEADS, OWNERS * CAP), 1, 4096)
        keyed = ranks * (OWNERS * CAP) + slot_ids[None, :]
        keyed = jnp.where(valid[sender][None, :], keyed, -1)
        return lax.top_k(keyed, TOPK)[1].astype(jnp.int32)
    picks = lax.map(one_sender, jnp.arange(OWNERS, dtype=jnp.int32))
    return picks.reshape(TOKENS, HEADS, TOPK)


def draw_scores(key, part):
    shape = (TOKENS, HEADS, TOPK)
    drawn = jax.random.normal(jax.random.fold_in(key, 1), shape, jnp.float32)
    return jnp.clip(2.0 * drawn, -8.0, 8.0).astype(jnp.float32)


def steps_of(own_key, shape, split, low, high):
    factor_of, own = 1.0, jax.random.fold_in(own_key, 6)
    for dim, shards_of in split:
        heights = jnp.exp(jax.random.uniform(jax.random.fold_in(own, dim), (shards_of,), jnp.float32, low / len(split), high / len(split)))
        factor_of = factor_of * jnp.repeat(heights, shape[dim] // shards_of).reshape([-1 if axis == dim else 1 for axis in range(len(shape))])
    return factor_of


def scatter_about(stream_key, extent, deviation, limit, cuts=(), held_as=jnp.bfloat16):
    values = jax.random.normal(stream_key, extent, jnp.float32) * deviation
    if len(cuts) > 0:
        values = steps_of(stream_key, extent, cuts, -0.22, 0.18) * values
    return jnp.clip(values, min=-limit, max=limit).astype(held_as)


def setup_inputs(seed: int = 0, part: int = 0) -> dict:
    key_of = jax.random.split(jax.random.key(seed), 6)
    own_keys = jax.random.split(jax.random.fold_in(key_of[5], part), 6)
    values = scatter_about(own_keys[0], (ROWS, D), 1.0, 6.0, ((0, 32), (1, 4)))
    cotangent = scatter_about(own_keys[1], (TOKENS, D), 1.0, 6.0, ((0, 32), (1, 4)))
    scores = draw_scores(jax.random.fold_in(jax.random.fold_in(key_of[5], part), 71), part)
    row_lists = draw_row_lists(jax.random.fold_in(jax.random.fold_in(key_of[5], part), 71), part)
    sel_slot = draw_sel_slot(jax.random.fold_in(jax.random.fold_in(key_of[5], part), 71), part)
    return dict(values=values, cotangent=cotangent, scores=scores, row_lists=row_lists, sel_slot=sel_slot)


def reference(values, cotangent, scores, row_lists, sel_slot):
    slot_count = OWNERS * CAP
    weights = jax.nn.softmax(scores.astype(jnp.float32), axis=-1)
    owner_base = jnp.arange(OWNERS, dtype=jnp.int32)[:, None] * ROWS_DEV

    def per_sender(carry, sender):
        lists = lax.dynamic_index_in_dim(row_lists, sender, 0, keepdims=False)
        global_rows = (owner_base + jnp.maximum(lists, 0)).reshape(-1).astype(jnp.int32)
        gathered = jnp.take(values, global_rows, axis=0)
        start = (sender * TOK_DEV).astype(jnp.int32)
        w_here = lax.dynamic_slice_in_dim(weights, start, TOK_DEV, 0)
        sel_here = lax.dynamic_slice_in_dim(sel_slot, start, TOK_DEV, 0)
        cot_here = lax.dynamic_slice_in_dim(cotangent, start, TOK_DEV, 0)
        chosen = sel_here.reshape(TOK_DEV, -1)
        flat_index = (jnp.arange(TOK_DEV, dtype=jnp.int32)[:, None] * slot_count + chosen).reshape(-1)
        combined = jnp.zeros((TOK_DEV * slot_count,), jnp.float32).at[flat_index].add(w_here.reshape(-1))
        combined = combined.reshape(TOK_DEV, slot_count).astype(jnp.bfloat16)
        out_here = jnp.dot(combined, gathered, preferred_element_type=jnp.float32).astype(jnp.bfloat16)
        products = jnp.dot(cot_here, gathered.T, preferred_element_type=jnp.float32)
        dots = jnp.take_along_axis(products, chosen, axis=1).reshape(w_here.shape)
        dscore = w_here * (dots - jnp.sum(w_here * dots, axis=-1, keepdims=True))
        contrib = jnp.dot(combined.T, cot_here, preferred_element_type=jnp.float32)
        target = jnp.where(lists.reshape(-1) >= 0, global_rows, ROWS).astype(jnp.int32)
        carry = carry.at[target].add(contrib)
        return carry, (out_here, dscore)

    start_grad = jnp.zeros((ROWS + 1, D), jnp.float32)
    grad_all, (outs, dscores) = lax.scan(per_sender, start_grad, jnp.arange(OWNERS, dtype=jnp.int32))
    mem_out = outs.reshape(TOKENS, D)
    grad_values = grad_all[:ROWS].astype(jnp.bfloat16)
    grad_scores = dscores.reshape(TOKENS, HEADS, TOPK)
    return mem_out, grad_values, grad_scores
```

```python
import jax
import jax.numpy as jnp
from jax import lax
from jax.sharding import PartitionSpec as P


def body(values, cotangent, scores, row_lists, sel_slot):
    owners = lax.axis_size("mem")
    tokens_here = cotangent.shape[0]
    cap_slots = row_lists.shape[2]
    slot_count = owners * cap_slots
    width = values.shape[1]
    table_rows = values.shape[0]
    highest = lax.Precision.HIGHEST
    weights = jax.nn.softmax(scores, axis=-1)
    chosen = sel_slot.reshape(tokens_here, -1)
    owner_of = chosen // cap_slots
    place_of = chosen % cap_slots
    owner_hot = (owner_of[..., None] == jnp.arange(owners, dtype=jnp.int32)[None, None, :]).astype(
        jnp.float32
    )
    place_hot = (
        place_of[..., None] == jnp.arange(cap_slots, dtype=jnp.int32)[None, None, :]
    ).astype(jnp.float32)
    weighted_owner = owner_hot * weights.reshape(tokens_here, -1)[..., None]
    combined = jnp.einsum(
        "tpo,tpc->toc",
        weighted_owner,
        place_hot,
        precision=highest,
        preferred_element_type=jnp.float32,
    )
    combined = combined.reshape(tokens_here, slot_count).astype(jnp.bfloat16)
    sums_here = lax.dot_general(
        combined, cotangent, (((0,), (0,)), ((), ())), preferred_element_type=jnp.float32
    ).astype(jnp.bfloat16)
    received = lax.all_to_all(
        sums_here.reshape(owners, cap_slots, width), "mem", 0, 0, tiled=True
    ).reshape(-1, width)
    asked = lax.all_to_all(row_lists[0], "mem", split_axis=0, concat_axis=0, tiled=True)
    row_hot = (
        asked.reshape(-1)[:, None] == jnp.arange(table_rows, dtype=jnp.int32)[None, :]
    ).astype(jnp.bfloat16)
    looked = jnp.dot(row_hot, values, preferred_element_type=jnp.float32).astype(jnp.bfloat16)
    replied = lax.all_to_all(
        looked.reshape(owners, cap_slots, width), "mem", 0, 0, tiled=True
    )
    gathered_rows = replied.reshape(slot_count, width)
    mem_out = jnp.dot(combined, gathered_rows, preferred_element_type=jnp.float32).astype(
        jnp.bfloat16
    )
    products = lax.dot_general(
        cotangent, gathered_rows, (((1,), (1,)), ((), ())), preferred_element_type=jnp.float32
    )
    products = products.reshape(tokens_here, owners, cap_slots)
    picked = jnp.einsum(
        "tpc,toc->tpo", place_hot, products, precision=highest, preferred_element_type=jnp.float32
    )
    partial_dots = jnp.sum(picked * owner_hot, axis=-1).reshape(weights.shape)
    full_dots = lax.psum(partial_dots.astype(jnp.bfloat16), "pipe").astype(jnp.float32)
    grad_scores = weights * (full_dots - jnp.sum(weights * full_dots, axis=-1, keepdims=True))
    contract = (((0,), (0,)), ((), ()))
    grad_full = lax.dot_general(row_hot, received, contract, preferred_element_type=jnp.float32)
    grad_values = grad_full.astype(jnp.bfloat16)
    return (mem_out, grad_values, grad_scores)


def solution(mesh):
    placed = (
        P(("dp", "mem"), "pipe"),
        P(("dp", "mem"), "pipe"),
        P(("dp", "mem"), None, None),
        P(("dp", "mem"), None, None),
        P(("dp", "mem"), None, None),
    )
    return jax.shard_map(
        body,
        mesh=mesh,
        in_specs=placed,
        out_specs=(
            P(("dp", "mem"), "pipe"),
            P(("dp", "mem"), "pipe"),
            P(("dp", "mem"), None, None),
        ),
        check_vma=False,
    )
```

```python
import jax
import jax.numpy as jnp
from jax import lax
from jax.sharding import PartitionSpec as P


def body(values, cotangent, scores, row_lists, sel_slot):
    owners = lax.axis_size("mem")
    tokens_here = cotangent.shape[0]
    cap_slots = row_lists.shape[2]
    slot_count = owners * cap_slots
    width = values.shape[1]
    table_rows = values.shape[0]
    highest = lax.Precision.HIGHEST
    all_cot = lax.all_gather(cotangent, "mem", axis=0, tiled=True)
    weights = jax.nn.softmax(scores, axis=-1)
    chosen = sel_slot.reshape(tokens_here, -1)
    owner_of = chosen // cap_slots
    place_of = chosen % cap_slots
    owner_hot = (owner_of[..., None] == jnp.arange(owners, dtype=jnp.int32)[None, None, :]).astype(
        jnp.float32
    )
    place_hot = (
        place_of[..., None] == jnp.arange(cap_slots, dtype=jnp.int32)[None, None, :]
    ).astype(jnp.float32)
    weighted_owner = owner_hot * weights.reshape(tokens_here, -1)[..., None]
    combined = jnp.einsum(
        "tpo,tpc->toc",
        weighted_owner,
        place_hot,
        precision=highest,
        preferred_element_type=jnp.float32,
    ).astype(jnp.bfloat16)
    asked = lax.all_to_all(row_lists[0], "mem", split_axis=0, concat_axis=0, tiled=True)
    asked = asked.reshape(owners, cap_slots)
    row_hot = (asked[..., None] == jnp.arange(table_rows, dtype=jnp.int32)).astype(jnp.bfloat16)
    looked = jnp.dot(
        row_hot.reshape(slot_count, table_rows), values, preferred_element_type=jnp.float32
    ).astype(jnp.bfloat16)
    replied = lax.all_to_all(
        looked.reshape(owners, cap_slots, width), "mem", 0, 0, tiled=True
    )
    gathered_rows = replied.reshape(slot_count, width)
    flat_comb = combined.reshape(tokens_here, slot_count)
    mem_out = jnp.dot(flat_comb, gathered_rows, preferred_element_type=jnp.float32).astype(
        jnp.bfloat16
    )
    products = lax.dot_general(
        cotangent, gathered_rows, (((1,), (1,)), ((), ())), preferred_element_type=jnp.float32
    )
    products = products.reshape(tokens_here, owners, cap_slots)
    picked = jnp.einsum(
        "tpc,toc->tpo", place_hot, products, precision=highest, preferred_element_type=jnp.float32
    )
    partial_dots = jnp.sum(picked * owner_hot, axis=-1).reshape(weights.shape)
    full_dots = lax.psum(partial_dots.astype(jnp.bfloat16), "pipe").astype(jnp.float32)
    grad_scores = weights * (full_dots - jnp.sum(weights * full_dots, axis=-1, keepdims=True))
    comb_in = lax.all_to_all(jnp.swapaxes(combined, 0, 1), "mem", 0, 0, tiled=True)
    comb_in = comb_in.reshape(owners, tokens_here, cap_slots)
    in_rows = jnp.einsum("stc,scr->str", comb_in, row_hot, preferred_element_type=jnp.float32)
    in_rows = in_rows.astype(jnp.bfloat16)
    grad_full = lax.dot_general(
        in_rows.reshape(slot_count, table_rows),
        all_cot,
        (((0,), (0,)), ((), ())),
        preferred_element_type=jnp.float32,
    )
    grad_values = grad_full.astype(jnp.bfloat16)
    return (mem_out, grad_values, grad_scores)


def solution(mesh):
    placed = (
        P(("dp", "mem"), "pipe"),
        P(("dp", "mem"), "pipe"),
        P(("dp", "mem"), None, None),
        P(("dp", "mem"), None, None),
        P(("dp", "mem"), None, None),
    )
    return jax.shard_map(
        body,
        mesh=mesh,
        in_specs=placed,
        out_specs=(
            P(("dp", "mem"), "pipe"),
            P(("dp", "mem"), "pipe"),
            P(("dp", "mem"), None, None),
        ),
        check_vma=False,
    )
```

```python
import jax
import jax.numpy as jnp
from jax import lax
from jax.sharding import PartitionSpec as P


def body(values, cotangent, scores, row_lists, sel_slot):
    owners = lax.axis_size("mem")
    tokens_here = cotangent.shape[0]
    cap_slots = row_lists.shape[2]
    slot_count = owners * cap_slots
    width = values.shape[1]
    table_rows = values.shape[0]
    highest = lax.Precision.HIGHEST
    all_cot = lax.all_gather(cotangent, "mem", axis=0, tiled=True)
    weights = jax.nn.softmax(scores, axis=-1)
    chosen = sel_slot.reshape(tokens_here, -1)
    owner_of = chosen // cap_slots
    place_of = chosen % cap_slots
    owner_hot = (owner_of[..., None] == jnp.arange(owners, dtype=jnp.int32)[None, None, :]).astype(
        jnp.float32
    )
    place_hot = (
        place_of[..., None] == jnp.arange(cap_slots, dtype=jnp.int32)[None, None, :]
    ).astype(jnp.float32)
    weighted_owner = owner_hot * weights.reshape(tokens_here, -1)[..., None]
    combined = jnp.einsum(
        "tpo,tpc->toc",
        weighted_owner,
        place_hot,
        precision=highest,
        preferred_element_type=jnp.float32,
    ).astype(jnp.bfloat16)
    asked = lax.all_to_all(row_lists[0], "mem", split_axis=0, concat_axis=0, tiled=True)
    asked = asked.reshape(owners, cap_slots)
    row_hot = (asked[..., None] == jnp.arange(table_rows, dtype=jnp.int32)).astype(jnp.bfloat16)
    looked = jnp.dot(
        row_hot.reshape(slot_count, table_rows), values, preferred_element_type=jnp.float32
    ).astype(jnp.bfloat16)
    replied = lax.all_to_all(
        looked.reshape(owners, cap_slots, width), "mem", 0, 0, tiled=True
    )
    gathered_rows = replied.reshape(slot_count, width)
    flat_comb = combined.reshape(tokens_here, slot_count)
    mem_out = jnp.dot(flat_comb, gathered_rows, preferred_element_type=jnp.float32).astype(
        jnp.bfloat16
    )
    products = lax.dot_general(
        cotangent, gathered_rows, (((1,), (1,)), ((), ())), preferred_element_type=jnp.float32
    )
    products = products.reshape(tokens_here, owners, cap_slots)
    picked = jnp.einsum(
        "tpc,toc->tpo", place_hot, products, precision=highest, preferred_element_type=jnp.float32
    )
    partial_dots = jnp.sum(picked * owner_hot, axis=-1).reshape(weights.shape)
    full_dots = lax.psum(partial_dots.astype(jnp.bfloat16), "pipe").astype(jnp.float32)
    grad_scores = weights * (full_dots - jnp.sum(weights * full_dots, axis=-1, keepdims=True))
    along_x = 4
    along_z = owners // along_x
    me = lax.axis_index("mem")
    my_z, my_x = me // along_x, me % along_x
    by_owner = jnp.swapaxes(combined, 0, 1).reshape(along_z, along_x, tokens_here, cap_slots)
    rolled = jnp.take(by_owner, (my_x + jnp.arange(along_x)) % along_x, axis=1)
    stage = [rolled[:, 0]]
    for shift in range(1, along_x):
        ring = [(i, (i // along_x) * along_x + (i + shift) % along_x) for i in range(owners)]
        stage.append(lax.ppermute(rolled[:, shift], "mem", ring))
    rolled = jnp.take(jnp.stack(stage, axis=1), (my_z + jnp.arange(along_z)) % along_z, axis=0)
    got = [rolled[0]]
    for shift in range(1, along_z):
        ring = [(i, (i + shift * along_x) % owners) for i in range(owners)]
        got.append(lax.ppermute(rolled[shift], "mem", ring))
    got = jnp.stack(got)
    from_z = (my_z - jnp.arange(along_z)) % along_z
    from_x = (my_x - jnp.arange(along_x)) % along_x
    comb_in = got[from_z[:, None], from_x[None, :]].reshape(owners, tokens_here, cap_slots)
    in_rows = jnp.einsum("stc,scr->str", comb_in, row_hot, preferred_element_type=jnp.float32)
    in_rows = in_rows.astype(jnp.bfloat16)
    grad_full = lax.dot_general(
        in_rows.reshape(slot_count, table_rows),
        all_cot,
        (((0,), (0,)), ((), ())),
        preferred_element_type=jnp.float32,
    )
    grad_values = grad_full.astype(jnp.bfloat16)
    return (mem_out, grad_values, grad_scores)


def solution(mesh):
    placed = (
        P(("dp", "mem"), "pipe"),
        P(("dp", "mem"), "pipe"),
        P(("dp", "mem"), None, None),
        P(("dp", "mem"), None, None),
        P(("dp", "mem"), None, None),
    )
    return jax.shard_map(
        body,
        mesh=mesh,
        in_specs=placed,
        out_specs=(
            P(("dp", "mem"), "pipe"),
            P(("dp", "mem"), "pipe"),
            P(("dp", "mem"), None, None),
        ),
        check_vma=False,
    )
```

```python
import jax
import jax.numpy as jnp
from jax import lax
from jax.sharding import PartitionSpec as P


def body(values, cotangent, scores, row_lists, sel_slot):
    owners = lax.axis_size("mem")
    tokens_here = cotangent.shape[0]
    cap_slots = row_lists.shape[2]
    slot_count = owners * cap_slots
    width = values.shape[1]
    table_rows = values.shape[0]
    highest = lax.Precision.HIGHEST
    all_cot = lax.all_gather(cotangent, "mem", axis=0, tiled=True)
    weights = jax.nn.softmax(scores, axis=-1)
    chosen = sel_slot.reshape(tokens_here, -1)
    owner_of = chosen // cap_slots
    place_of = chosen % cap_slots
    owner_hot = (owner_of[..., None] == jnp.arange(owners, dtype=jnp.int32)[None, None, :]).astype(
        jnp.float32
    )
    place_hot = (
        place_of[..., None] == jnp.arange(cap_slots, dtype=jnp.int32)[None, None, :]
    ).astype(jnp.float32)
    weighted_owner = owner_hot * weights.reshape(tokens_here, -1)[..., None]
    combined = jnp.einsum(
        "tpo,tpc->toc",
        weighted_owner,
        place_hot,
        precision=highest,
        preferred_element_type=jnp.float32,
    ).astype(jnp.bfloat16)
    digit = 32
    shifted = row_lists[0] + 1
    digits = jnp.stack([shifted // digit, shifted % digit], axis=1).astype(jnp.bfloat16)
    outgoing = jnp.concatenate([jnp.swapaxes(combined, 0, 1), digits], axis=1)
    incoming = lax.all_to_all(outgoing, "mem", 0, 0, tiled=True)
    comb_in = incoming[:, :tokens_here]
    got_digits = incoming[:, tokens_here:].astype(jnp.int32)
    asked = got_digits[:, 0] * digit + got_digits[:, 1] - 1
    row_hot = (asked[..., None] == jnp.arange(table_rows, dtype=jnp.int32)).astype(jnp.bfloat16)
    looked = jnp.dot(
        row_hot.reshape(slot_count, table_rows), values, preferred_element_type=jnp.float32
    ).astype(jnp.bfloat16)
    replied = lax.all_to_all(
        looked.reshape(owners, cap_slots, width), "mem", 0, 0, tiled=True
    )
    gathered_rows = replied.reshape(slot_count, width)
    flat_comb = combined.reshape(tokens_here, slot_count)
    mem_out = jnp.dot(flat_comb, gathered_rows, preferred_element_type=jnp.float32).astype(
        jnp.bfloat16
    )
    products = lax.dot_general(
        cotangent, gathered_rows, (((1,), (1,)), ((), ())), preferred_element_type=jnp.float32
    )
    products = products.reshape(tokens_here, owners, cap_slots)
    picked = jnp.einsum(
        "tpc,toc->tpo", place_hot, products, precision=highest, preferred_element_type=jnp.float32
    )
    partial_dots = jnp.sum(picked * owner_hot, axis=-1).reshape(weights.shape)
    full_dots = lax.psum(partial_dots.astype(jnp.bfloat16), "pipe").astype(jnp.float32)
    grad_scores = weights * (full_dots - jnp.sum(weights * full_dots, axis=-1, keepdims=True))
    in_rows = jnp.einsum("stc,scr->str", comb_in, row_hot, preferred_element_type=jnp.float32)
    in_rows = in_rows.astype(jnp.bfloat16)
    grad_full = lax.dot_general(
        in_rows.reshape(slot_count, table_rows),
        all_cot,
        (((0,), (0,)), ((), ())),
        preferred_element_type=jnp.float32,
    )
    grad_values = grad_full.astype(jnp.bfloat16)
    return (mem_out, grad_values, grad_scores)


def solution(mesh):
    placed = (
        P(("dp", "mem"), "pipe"),
        P(("dp", "mem"), "pipe"),
        P(("dp", "mem"), None, None),
        P(("dp", "mem"), None, None),
        P(("dp", "mem"), None, None),
    )
    return jax.shard_map(
        body,
        mesh=mesh,
        in_specs=placed,
        out_specs=(
            P(("dp", "mem"), "pipe"),
            P(("dp", "mem"), "pipe"),
            P(("dp", "mem"), None, None),
        ),
        check_vma=False,
    )
```

```python
import jax
import jax.numpy as jnp
from jax import lax
from jax.sharding import PartitionSpec as P


MEM = ("mz", "mx")


def body(values, cotangent, scores, row_lists, sel_slot):
    owners = lax.axis_size(MEM)
    tokens_here = cotangent.shape[0]
    cap_slots = row_lists.shape[2]
    slot_count = owners * cap_slots
    width = values.shape[1]
    table_rows = values.shape[0]
    highest = lax.Precision.HIGHEST
    along_z = lax.all_gather(cotangent, "mz", axis=0, tiled=True)
    all_cot = lax.all_gather(along_z, "mx", axis=0, tiled=True)
    all_cot = all_cot.reshape(lax.axis_size("mx"), lax.axis_size("mz"), -1, all_cot.shape[-1])
    all_cot = jnp.swapaxes(all_cot, 0, 1).reshape(-1, all_cot.shape[-1])
    weights = jax.nn.softmax(scores, axis=-1)
    chosen = sel_slot.reshape(tokens_here, -1)
    owner_of = chosen // cap_slots
    place_of = chosen % cap_slots
    owner_hot = (owner_of[..., None] == jnp.arange(owners, dtype=jnp.int32)[None, None, :]).astype(
        jnp.float32
    )
    place_hot = (
        place_of[..., None] == jnp.arange(cap_slots, dtype=jnp.int32)[None, None, :]
    ).astype(jnp.float32)
    weighted_owner = owner_hot * weights.reshape(tokens_here, -1)[..., None]
    combined = jnp.einsum(
        "tpo,tpc->toc",
        weighted_owner,
        place_hot,
        precision=highest,
        preferred_element_type=jnp.float32,
    ).astype(jnp.bfloat16)
    asked = lax.all_to_all(row_lists[0], MEM, split_axis=0, concat_axis=0, tiled=True)
    asked = asked.reshape(owners, cap_slots)
    row_hot = (asked[..., None] == jnp.arange(table_rows, dtype=jnp.int32)).astype(jnp.bfloat16)
    looked = jnp.dot(
        row_hot.reshape(slot_count, table_rows), values, preferred_element_type=jnp.float32
    ).astype(jnp.bfloat16)
    replied = lax.all_to_all(
        looked.reshape(owners, cap_slots, width), MEM, 0, 0, tiled=True
    )
    gathered_rows = replied.reshape(slot_count, width)
    flat_comb = combined.reshape(tokens_here, slot_count)
    mem_out = jnp.dot(flat_comb, gathered_rows, preferred_element_type=jnp.float32).astype(
        jnp.bfloat16
    )
    products = lax.dot_general(
        cotangent, gathered_rows, (((1,), (1,)), ((), ())), preferred_element_type=jnp.float32
    )
    products = products.reshape(tokens_here, owners, cap_slots)
    picked = jnp.einsum(
        "tpc,toc->tpo", place_hot, products, precision=highest, preferred_element_type=jnp.float32
    )
    partial_dots = jnp.sum(picked * owner_hot, axis=-1).reshape(weights.shape)
    full_dots = lax.psum(partial_dots.astype(jnp.bfloat16), "pipe").astype(jnp.float32)
    grad_scores = weights * (full_dots - jnp.sum(weights * full_dots, axis=-1, keepdims=True))
    comb_in = lax.all_to_all(jnp.swapaxes(combined, 0, 1), MEM, 0, 0, tiled=True)
    comb_in = comb_in.reshape(owners, tokens_here, cap_slots)
    in_rows = jnp.einsum("stc,scr->str", comb_in, row_hot, preferred_element_type=jnp.float32)
    in_rows = in_rows.astype(jnp.bfloat16)
    grad_full = lax.dot_general(
        in_rows.reshape(slot_count, table_rows),
        all_cot,
        (((0,), (0,)), ((), ())),
        preferred_element_type=jnp.float32,
    )
    grad_values = grad_full.astype(jnp.bfloat16)
    return (mem_out, grad_values, grad_scores)


def solution(mesh):
    z_size = 8
    devices = mesh.devices.reshape((z_size, -1) + mesh.devices.shape[1:])
    mesh = jax.sharding.Mesh(devices, ("mz", "mx") + mesh.axis_names[1:])
    placed = (
        P(("dp",) + MEM, "pipe"),
        P(("dp",) + MEM, "pipe"),
        P(("dp",) + MEM, None, None),
        P(("dp",) + MEM, None, None),
        P(("dp",) + MEM, None, None),
    )
    return jax.shard_map(
        body,
        mesh=mesh,
        in_specs=placed,
        out_specs=(
            P(("dp",) + MEM, "pipe"),
            P(("dp",) + MEM, "pipe"),
            P(("dp",) + MEM, None, None),
        ),
        check_vma=False,
    )
```

```python
import jax
import jax.numpy as jnp
from jax import lax
from jax.sharding import PartitionSpec as P


MEM = ("mz", "mx")


def body(values, cotangent, scores, row_lists, sel_slot):
    owners = lax.axis_size(MEM)
    tokens_here = cotangent.shape[0]
    cap_slots = row_lists.shape[2]
    slot_count = owners * cap_slots
    width = values.shape[1]
    table_rows = values.shape[0]
    highest = lax.Precision.HIGHEST
    along_z = lax.all_gather(cotangent, "mz", axis=0, tiled=True)
    all_cot = lax.all_gather(along_z, "mx", axis=0, tiled=True)
    x_size, z_size = lax.axis_size("mx"), lax.axis_size("mz")
    gathered_order = [z * x_size + x for x in range(x_size) for z in range(z_size)]
    weights = jax.nn.softmax(scores, axis=-1)
    chosen = sel_slot.reshape(tokens_here, -1)
    owner_of = chosen // cap_slots
    place_of = chosen % cap_slots
    owner_hot = (owner_of[..., None] == jnp.arange(owners, dtype=jnp.int32)[None, None, :]).astype(
        jnp.float32
    )
    place_hot = (
        place_of[..., None] == jnp.arange(cap_slots, dtype=jnp.int32)[None, None, :]
    ).astype(jnp.float32)
    weighted_owner = owner_hot * weights.reshape(tokens_here, -1)[..., None]
    combined = jnp.einsum(
        "tpo,tpc->toc",
        weighted_owner,
        place_hot,
        precision=highest,
        preferred_element_type=jnp.float32,
    ).astype(jnp.bfloat16)
    asked = lax.all_to_all(row_lists[0], MEM, split_axis=0, concat_axis=0, tiled=True)
    asked = asked.reshape(owners, cap_slots)
    row_hot = (asked[..., None] == jnp.arange(table_rows, dtype=jnp.int32)).astype(jnp.bfloat16)
    looked = jnp.dot(
        row_hot.reshape(slot_count, table_rows), values, preferred_element_type=jnp.float32
    ).astype(jnp.bfloat16)
    replied = lax.all_to_all(
        looked.reshape(owners, cap_slots, width), MEM, 0, 0, tiled=True
    )
    gathered_rows = replied.reshape(slot_count, width)
    flat_comb = combined.reshape(tokens_here, slot_count)
    mem_out = jnp.dot(flat_comb, gathered_rows, preferred_element_type=jnp.float32).astype(
        jnp.bfloat16
    )
    products = lax.dot_general(
        cotangent, gathered_rows, (((1,), (1,)), ((), ())), preferred_element_type=jnp.float32
    )
    products = products.reshape(tokens_here, owners, cap_slots)
    upper = products.astype(jnp.bfloat16)
    lower = (products - upper.astype(jnp.float32)).astype(jnp.bfloat16)
    place_bf = place_hot.astype(jnp.bfloat16)
    picked = jnp.einsum("tpc,toc->tpo", place_bf, upper, preferred_element_type=jnp.float32)
    picked = picked + jnp.einsum("tpc,toc->tpo", place_bf, lower, preferred_element_type=jnp.float32)
    partial_dots = jnp.sum(picked * owner_hot, axis=-1).reshape(weights.shape)
    full_dots = lax.psum(partial_dots.astype(jnp.bfloat16), "pipe").astype(jnp.float32)
    grad_scores = weights * (full_dots - jnp.sum(weights * full_dots, axis=-1, keepdims=True))
    comb_in = lax.all_to_all(jnp.swapaxes(combined, 0, 1), MEM, 0, 0, tiled=True)
    comb_in = comb_in.reshape(owners, tokens_here, cap_slots)
    comb_in = comb_in[jnp.array(gathered_order)]
    asked_in = asked[jnp.array(gathered_order)]
    hot_in = (asked_in[..., None] == jnp.arange(table_rows, dtype=jnp.int32)).astype(jnp.bfloat16)
    in_rows = jnp.einsum("stc,scr->str", comb_in, hot_in, preferred_element_type=jnp.float32)
    in_rows = in_rows.astype(jnp.bfloat16)
    grad_full = lax.dot_general(
        in_rows.reshape(slot_count, table_rows),
        all_cot,
        (((0,), (0,)), ((), ())),
        preferred_element_type=jnp.float32,
    )
    grad_values = grad_full.astype(jnp.bfloat16)
    return (mem_out, grad_values, grad_scores)


def solution(mesh):
    z_size = 8
    devices = mesh.devices.reshape((z_size, -1) + mesh.devices.shape[1:])
    mesh = jax.sharding.Mesh(devices, ("mz", "mx") + mesh.axis_names[1:])
    placed = (
        P(("dp",) + MEM, "pipe"),
        P(("dp",) + MEM, "pipe"),
        P(("dp",) + MEM, None, None),
        P(("dp",) + MEM, None, None),
        P(("dp",) + MEM, None, None),
    )
    return jax.shard_map(
        body,
        mesh=mesh,
        in_specs=placed,
        out_specs=(
            P(("dp",) + MEM, "pipe"),
            P(("dp",) + MEM, "pipe"),
            P(("dp",) + MEM, None, None),
        ),
        check_vma=False,
    )
```

```python
import jax
import jax.numpy as jnp
from jax import lax
from jax.sharding import PartitionSpec as P


MEM = ("mz", "mx")


def body(values, cotangent, scores, row_lists, sel_slot):
    owners = lax.axis_size(MEM)
    tokens_here = cotangent.shape[0]
    cap_slots = row_lists.shape[2]
    slot_count = owners * cap_slots
    width = values.shape[1]
    table_rows = values.shape[0]
    highest = lax.Precision.HIGHEST
    along_z = lax.all_gather(cotangent, "mz", axis=0, tiled=True)
    all_cot = lax.all_gather(along_z, "mx", axis=0, tiled=True)
    x_size, z_size = lax.axis_size("mx"), lax.axis_size("mz")
    gathered_order = [z * x_size + x for x in range(x_size) for z in range(z_size)]
    weights = jax.nn.softmax(scores, axis=-1)
    chosen = sel_slot.reshape(tokens_here, -1)
    owner_of = chosen // cap_slots
    place_of = chosen % cap_slots
    owner_hot = (owner_of[..., None] == jnp.arange(owners, dtype=jnp.int32)[None, None, :]).astype(
        jnp.float32
    )
    place_hot = (
        place_of[..., None] == jnp.arange(cap_slots, dtype=jnp.int32)[None, None, :]
    ).astype(jnp.float32)
    weighted_owner = owner_hot * weights.reshape(tokens_here, -1)[..., None]
    combined = jnp.einsum(
        "tpo,tpc->toc",
        weighted_owner,
        place_hot,
        precision=highest,
        preferred_element_type=jnp.float32,
    ).astype(jnp.bfloat16)
    asked = lax.all_to_all(row_lists[0], MEM, split_axis=0, concat_axis=0, tiled=True)
    asked = asked.reshape(owners, cap_slots)
    row_hot = (asked[..., None] == jnp.arange(table_rows, dtype=jnp.int32)).astype(jnp.bfloat16)
    looked = jnp.dot(
        row_hot.reshape(slot_count, table_rows), values, preferred_element_type=jnp.float32
    ).astype(jnp.bfloat16)
    replied = lax.all_to_all(
        looked.reshape(owners, cap_slots, width), MEM, 0, 0, tiled=True
    )
    gathered_rows = replied.reshape(slot_count, width)
    flat_comb = combined.reshape(tokens_here, slot_count)
    mem_out = jnp.dot(flat_comb, gathered_rows, preferred_element_type=jnp.float32).astype(
        jnp.bfloat16
    )
    products = lax.dot_general(
        cotangent, gathered_rows, (((1,), (1,)), ((), ())), preferred_element_type=jnp.float32
    )
    products = products.reshape(tokens_here, owners, cap_slots)
    picked = jnp.einsum(
        "tpc,toc->tpo", place_hot, products, precision=highest, preferred_element_type=jnp.float32
    )
    partial_dots = jnp.sum(picked * owner_hot, axis=-1).reshape(weights.shape)
    flat_dots = partial_dots.reshape(tokens_here, -1)
    room = jnp.zeros((tokens_here, 3 * flat_dots.shape[1]), jnp.float32)
    padded = jnp.concatenate([flat_dots, room], axis=1)
    gathered = lax.all_gather(padded, "pipe", axis=0)[:, :, : flat_dots.shape[1]]
    full_dots = jnp.sum(gathered, axis=0).reshape(weights.shape)
    grad_scores = weights * (full_dots - jnp.sum(weights * full_dots, axis=-1, keepdims=True))
    comb_in = lax.all_to_all(jnp.swapaxes(combined, 0, 1), MEM, 0, 0, tiled=True)
    comb_in = comb_in.reshape(owners, tokens_here, cap_slots)
    comb_in = comb_in[jnp.array(gathered_order)]
    asked_in = asked[jnp.array(gathered_order)]
    hot_in = (asked_in[..., None] == jnp.arange(table_rows, dtype=jnp.int32)).astype(jnp.bfloat16)
    in_rows = jnp.einsum("stc,scr->str", comb_in, hot_in, preferred_element_type=jnp.float32)
    in_rows = in_rows.astype(jnp.bfloat16)
    grad_full = lax.dot_general(
        in_rows.reshape(slot_count, table_rows),
        all_cot,
        (((0,), (0,)), ((), ())),
        preferred_element_type=jnp.float32,
    )
    grad_values = grad_full.astype(jnp.bfloat16)
    return (mem_out, grad_values, grad_scores)


def solution(mesh):
    z_size = 8
    devices = mesh.devices.reshape((z_size, -1) + mesh.devices.shape[1:])
    mesh = jax.sharding.Mesh(devices, ("mz", "mx") + mesh.axis_names[1:])
    placed = (
        P(("dp",) + MEM, "pipe"),
        P(("dp",) + MEM, "pipe"),
        P(("dp",) + MEM, None, None),
        P(("dp",) + MEM, None, None),
        P(("dp",) + MEM, None, None),
    )
    return jax.shard_map(
        body,
        mesh=mesh,
        in_specs=placed,
        out_specs=(
            P(("dp",) + MEM, "pipe"),
            P(("dp",) + MEM, "pipe"),
            P(("dp",) + MEM, None, None),
        ),
        check_vma=False,
    )
```

```python
import jax
import jax.numpy as jnp
from jax import lax
from jax.sharding import PartitionSpec as P


MEM = ("mz", "mx")


def body(values, cotangent, scores, row_lists, sel_slot):
    owners = lax.axis_size(MEM)
    tokens_here = cotangent.shape[0]
    cap_slots = row_lists.shape[2]
    slot_count = owners * cap_slots
    width = values.shape[1]
    table_rows = values.shape[0]
    highest = lax.Precision.HIGHEST
    along_z = lax.all_gather(cotangent, "mz", axis=0, tiled=True)
    all_cot = lax.all_gather(along_z, "mx", axis=0, tiled=True)
    x_size, z_size = lax.axis_size("mx"), lax.axis_size("mz")
    gathered_order = [z * x_size + x for x in range(x_size) for z in range(z_size)]
    weights = jax.nn.softmax(scores, axis=-1)
    chosen = sel_slot.reshape(tokens_here, -1)
    owner_of = chosen // cap_slots
    place_of = chosen % cap_slots
    owner_hot = (owner_of[..., None] == jnp.arange(owners, dtype=jnp.int32)[None, None, :]).astype(
        jnp.float32
    )
    place_hot = (
        place_of[..., None] == jnp.arange(cap_slots, dtype=jnp.int32)[None, None, :]
    ).astype(jnp.float32)
    weighted_owner = owner_hot * weights.reshape(tokens_here, -1)[..., None]
    combined = jnp.einsum(
        "tpo,tpc->toc",
        weighted_owner,
        place_hot,
        precision=highest,
        preferred_element_type=jnp.float32,
    ).astype(jnp.bfloat16)
    asked = lax.all_to_all(row_lists[0], MEM, split_axis=0, concat_axis=0, tiled=True)
    asked = asked.reshape(owners, cap_slots)
    row_hot = (asked[..., None] == jnp.arange(table_rows, dtype=jnp.int32)).astype(jnp.bfloat16)
    looked = jnp.dot(
        row_hot.reshape(slot_count, table_rows), values, preferred_element_type=jnp.float32
    ).astype(jnp.bfloat16)
    replied = lax.all_to_all(
        looked.reshape(owners, cap_slots, width), MEM, 0, 0, tiled=True
    )
    gathered_rows = replied.reshape(slot_count, width)
    flat_comb = combined.reshape(tokens_here, slot_count)
    mem_out = jnp.dot(flat_comb, gathered_rows, preferred_element_type=jnp.float32).astype(
        jnp.bfloat16
    )
    products = lax.dot_general(
        cotangent, gathered_rows, (((1,), (1,)), ((), ())), preferred_element_type=jnp.float32
    )
    products = products.reshape(tokens_here, owners, cap_slots)
    picked = jnp.einsum(
        "tpc,toc->tpo", place_hot, products, precision=highest, preferred_element_type=jnp.float32
    )
    partial_dots = jnp.sum(picked * owner_hot, axis=-1).reshape(weights.shape)
    flat_dots = partial_dots.reshape(tokens_here, -1)
    room = jnp.zeros((tokens_here, 3 * flat_dots.shape[1]), jnp.float32)
    padded = jnp.concatenate([flat_dots, room], axis=1)
    gathered = lax.all_gather(padded, "pipe", axis=0)[:, :, : flat_dots.shape[1]]
    full_dots = jnp.sum(gathered, axis=0).reshape(weights.shape)
    grad_scores = weights * (full_dots - jnp.sum(weights * full_dots, axis=-1, keepdims=True))
    comb_in = lax.all_to_all(jnp.swapaxes(combined, 0, 1), MEM, 0, 0, tiled=True)
    comb_in = comb_in.reshape(owners, tokens_here, cap_slots)
    comb_in = comb_in[jnp.array(gathered_order)]
    asked_in = asked[jnp.array(gathered_order)]
    hot_in = (asked_in[..., None] == jnp.arange(table_rows, dtype=jnp.int32)).astype(jnp.bfloat16)
    in_rows = jnp.einsum("stc,scr->rst", comb_in, hot_in, preferred_element_type=jnp.float32)
    in_rows = in_rows.astype(jnp.bfloat16)
    grad_full = jnp.dot(
        in_rows.reshape(table_rows, slot_count), all_cot, preferred_element_type=jnp.float32
    )
    grad_values = grad_full.astype(jnp.bfloat16)
    return (mem_out, grad_values, grad_scores)


def solution(mesh):
    z_size = 8
    devices = mesh.devices.reshape((z_size, -1) + mesh.devices.shape[1:])
    mesh = jax.sharding.Mesh(devices, ("mz", "mx") + mesh.axis_names[1:])
    placed = (
        P(("dp",) + MEM, "pipe"),
        P(("dp",) + MEM, "pipe"),
        P(("dp",) + MEM, None, None),
        P(("dp",) + MEM, None, None),
        P(("dp",) + MEM, None, None),
    )
    return jax.shard_map(
        body,
        mesh=mesh,
        in_specs=placed,
        out_specs=(
            P(("dp",) + MEM, "pipe"),
            P(("dp",) + MEM, "pipe"),
            P(("dp",) + MEM, None, None),
        ),
        check_vma=False,
    )
```

```python
import jax
import jax.numpy as jnp
from jax import lax
from jax.sharding import PartitionSpec as P


MEM = ("mz", "mx")


def body(values, cotangent, scores, row_lists, sel_slot):
    owners = lax.axis_size(MEM)
    tokens_here = cotangent.shape[0]
    cap_slots = row_lists.shape[2]
    slot_count = owners * cap_slots
    width = values.shape[1]
    table_rows = values.shape[0]
    highest = lax.Precision.HIGHEST
    along_z = lax.all_gather(cotangent, "mz", axis=0, tiled=True)
    all_cot = lax.all_gather(along_z, "mx", axis=0, tiled=True)
    x_size, z_size = lax.axis_size("mx"), lax.axis_size("mz")
    gathered_order = [z * x_size + x for x in range(x_size) for z in range(z_size)]
    weights = jax.nn.softmax(scores, axis=-1)
    chosen = sel_slot.reshape(tokens_here, -1)
    owner_of = chosen // cap_slots
    place_of = chosen % cap_slots
    owner_hot = (owner_of[..., None] == jnp.arange(owners, dtype=jnp.int32)[None, None, :]).astype(
        jnp.float32
    )
    place_hot = (
        place_of[..., None] == jnp.arange(cap_slots, dtype=jnp.int32)[None, None, :]
    ).astype(jnp.float32)
    weighted_owner = owner_hot * weights.reshape(tokens_here, -1)[..., None]
    combined = jnp.einsum(
        "tpo,tpc->toc",
        weighted_owner,
        place_hot,
        precision=highest,
        preferred_element_type=jnp.float32,
    ).astype(jnp.bfloat16)
    asked = lax.all_to_all(row_lists[0], MEM, split_axis=0, concat_axis=0, tiled=True)
    asked = asked.reshape(owners, cap_slots)
    row_hot = (asked[..., None] == jnp.arange(table_rows, dtype=jnp.int32)).astype(jnp.bfloat16)
    looked = jnp.dot(
        row_hot.reshape(slot_count, table_rows), values, preferred_element_type=jnp.float32
    ).astype(jnp.bfloat16)
    replied = lax.all_to_all(
        looked.reshape(owners, cap_slots, width), MEM, 0, 0, tiled=True
    )
    gathered_rows = replied.reshape(slot_count, width)
    flat_comb = combined.reshape(tokens_here, slot_count)
    mem_out = jnp.dot(flat_comb, gathered_rows, preferred_element_type=jnp.float32).astype(
        jnp.bfloat16
    )
    products = lax.dot_general(
        cotangent, gathered_rows, (((1,), (1,)), ((), ())), preferred_element_type=jnp.float32
    )
    products = products.reshape(tokens_here, owners, cap_slots)
    picked = jnp.einsum(
        "tpc,toc->tpo",
        place_hot.astype(jnp.bfloat16),
        products.astype(jnp.bfloat16),
        preferred_element_type=jnp.float32,
    )
    partial_dots = jnp.sum(picked * owner_hot, axis=-1).reshape(weights.shape)
    flat_dots = partial_dots.reshape(tokens_here, -1)
    room = jnp.zeros((tokens_here, 3 * flat_dots.shape[1]), jnp.float32)
    padded = jnp.concatenate([flat_dots, room], axis=1)
    gathered = lax.all_gather(padded, "pipe", axis=0)[:, :, : flat_dots.shape[1]]
    full_dots = jnp.sum(gathered, axis=0).reshape(weights.shape)
    grad_scores = weights * (full_dots - jnp.sum(weights * full_dots, axis=-1, keepdims=True))
    comb_in = lax.all_to_all(jnp.swapaxes(combined, 0, 1), MEM, 0, 0, tiled=True)
    comb_in = comb_in.reshape(owners, tokens_here, cap_slots)
    comb_in = comb_in[jnp.array(gathered_order)]
    asked_in = asked[jnp.array(gathered_order)]
    hot_in = (asked_in[..., None] == jnp.arange(table_rows, dtype=jnp.int32)).astype(jnp.bfloat16)
    in_rows = jnp.einsum("stc,scr->rst", comb_in, hot_in, preferred_element_type=jnp.float32)
    in_rows = in_rows.astype(jnp.bfloat16)
    grad_full = jnp.dot(
        in_rows.reshape(table_rows, slot_count), all_cot, preferred_element_type=jnp.float32
    )
    grad_values = grad_full.astype(jnp.bfloat16)
    return (mem_out, grad_values, grad_scores)


def solution(mesh):
    z_size = 8
    devices = mesh.devices.reshape((z_size, -1) + mesh.devices.shape[1:])
    mesh = jax.sharding.Mesh(devices, ("mz", "mx") + mesh.axis_names[1:])
    placed = (
        P(("dp",) + MEM, "pipe"),
        P(("dp",) + MEM, "pipe"),
        P(("dp",) + MEM, None, None),
        P(("dp",) + MEM, None, None),
        P(("dp",) + MEM, None, None),
    )
    return jax.shard_map(
        body,
        mesh=mesh,
        in_specs=placed,
        out_specs=(
            P(("dp",) + MEM, "pipe"),
            P(("dp",) + MEM, "pipe"),
            P(("dp",) + MEM, None, None),
        ),
        check_vma=False,
    )
```
